1024 devices in a mesh: dp: 32 (over z, core), expert: 32 (over y, x).
Axes of the slice: x: 4, y: 8, z: 16, core: 2. Of those that a mesh axis runs over, the one named last changes fastest.
Arguments:
- route_ids: int32 [131072, 2], P(('dp', 'expert')), may hold values from 0 to 31, all different within a row; in each aligned block of 128 rows (0 to 127, 128 to 255, ...) at most 10 rows name the same one
- gate_values: float32 [131072, 2], P(('dp', 'expert')), may hold values from 0.1 to 1
- out_grad: bfloat16 [131072, 2048], P(('dp', 'expert')), may hold values from -4 to 4
- down_weight: bfloat16 [32, 768, 2048], P('expert'), may hold values from -0.21875 to 0.21875
- hidden: bfloat16 [32, 32, 32, 10, 768], P('dp', 'expert'), may hold values from -6 to 6
Outputs:
- mixed_out: bfloat16 [131072, 2048], P(('dp', 'expert'))
- gate_grad: float32 [131072, 2], P(('dp', 'expert'))
- hidden_grad: bfloat16 [32, 32, 32, 10, 768], P('dp', 'expert')
- weight_grad: float32 [32, 768, 2048], P('expert', 'dp')
The draws below stay inside these ranges and needn't reach their ends.
Inputs may be any that keep to these rules, and one draw needn't show every extreme that they name: `route_ids`: each row names 2 different experts. Among the rows of one device no expert is named by more than 10 rows, and in every draw some device names some expert exactly 10 times.
All inputs are finite; a program needn't handle non-finite values.
Results may differ from the reference program's by a relative error of at most 0.0049.
Values may be sent and summed in bfloat16 or wider, within the bound.
No kernel may reach another device: no remote copies, remote signals or barrier semaphores. Data moves between devices by JAX's collectives and lax.ppermute only.
A program may use at most 64 MiB of HBM per device.

```python
import math
import jax
import jax.numpy as jnp
import numpy as np
from jax import lax

D_W = 2048
H = 768
TOP = 2
TOK_DEV = 128
EXPERTS = 32
CAP = 10
TOKENS = 131072
N_DP = 32
N_EXPERT = 32


def spiked(values, stream_key, source, target, blocks, factor):
    def block_of(position):
        return (jnp.arange(values.shape[position]) // (values.shape[position] // blocks)).reshape((-1,) + (1,) * (values.ndim - 1 - position))

    first = jax.random.permutation(stream_key, blocks)[block_of(target)]
    other_side = (block_of(target) + blocks // 2) % blocks
    return jnp.where((block_of(source) == first) | (block_of(source) == other_side), factor * values, values)


def block_levels(key, shape, cuts, low, top_value):
    level, own = 1.0, jax.random.fold_in(key, 6)
    for dim, shards_of in cuts:
        steps = jnp.exp(jax.random.uniform(jax.random.fold_in(own, dim), (shards_of,), jnp.float32, low / len(cuts), top_value / len(cuts)))
        level = level * jnp.repeat(steps, shape[dim] // shards_of).reshape([-1 if axis == dim else 1 for axis in range(len(shape))])
    return level


def shared_out(own_key, own, number, rows, count, top, limit, lean):
    ranking = jax.random.permutation(own_key, count)
    heavy_load, common = portions_of(count, rows * top, limit, lean, True), portions_of(count, rows * top, limit, lean, False)
    places = jnp.arange(count)

    def named(lengths, offset_by):
        used = int((lengths > 0).sum())
        fixed = max(1, used // 4)
        moved = fixed + (places - fixed + offset_by * (used - fixed)) % max(1, count - fixed)
        return jnp.zeros((count,), jnp.int32).at[ranking[jnp.where(places < fixed, places, moved)]].set(jnp.asarray(lengths, jnp.int32))

    lengths = jnp.where(number % 4 == 0, named(heavy_load, number // 4), named(common, number - number // 4 - 1))
    mixed = jax.random.permutation(jax.random.fold_in(own, 3), count)
    donor, receiver = mixed[0:count // 2 * 2:2], mixed[1:count // 2 * 2:2]
    margin = jnp.minimum(lengths[donor] - 1, limit - lengths[receiver]) // 2
    margin = jnp.where((donor == ranking[0]) | (receiver == ranking[0]) | (lengths[receiver] == 0), 0, jnp.maximum(margin, 0))
    moved = jax.random.randint(jax.random.fold_in(own, 4), (count // 2,), 0, 1 << 20) % (margin + 1)
    lengths = lengths.at[donor].add(-moved).at[receiver].add(moved)
    members = jnp.searchsorted(jnp.cumsum(lengths), jnp.arange(rows * top), side="right").astype(jnp.int32)
    grid = members.reshape(top, rows).T
    grid = grid[jax.random.permutation(jax.random.fold_in(own, 1), rows)]
    offset_by = jax.random.randint(jax.random.fold_in(own, 2), (rows, 1), 0, top)
    return jnp.take_along_axis(grid, (jnp.arange(top)[None, :] + offset_by) % top, axis=1)


def portions_of(number_of, total, bound, lean, full):
    weights = [(1 << 20) // math.isqrt(grade ** lean) + 1 for grade in range(1, number_of + 1)]
    largest = bound if full else min(bound, max(-(-total // number_of), total * weights[0] // sum(weights)))
    least = 1 if total - largest >= number_of - 1 else 0
    holding, surplus = [largest] + [least] * (number_of - 1), total - largest - least * (number_of - 1)
    while surplus > 0:
        movable = [i for i in range(1, number_of) if holding[i] < largest] or [i for i in range(1, number_of) if holding[i] < bound]
        whole, left = sum([weights[i] for i in movable]), surplus
        for i in movable:
            extra = min(bound - holding[i], max(1, left * weights[i] // whole), surplus)
            holding[i] = holding[i] + extra
            surplus = surplus - extra
    return np.array(holding)


def bell_draw(rng, dims, scale, reach, pieces=(), held_as=jnp.bfloat16):
    entries = jax.random.normal(rng, dims, jnp.float32) * scale
    if len(pieces) > 0:
        entries = block_levels(rng, dims, pieces, -0.22, 0.18) * entries
    return jnp.clip(entries, min=-reach, max=reach).astype(held_as)


def gaussian_with(key, extent, width, most, shards, heavy, held_as=jnp.bfloat16):
    array = width * jax.random.normal(key, extent, jnp.float32)
    if shards:
        array = array * block_levels(key, extent, shards, -0.22, 0.18)
    return jnp.clip(spiked(array, jax.random.fold_in(key, 3), *heavy), -most, most).astype(held_as)


def setup_inputs(seed: int = 0) -> dict:
    key_of = jax.random.split(jax.random.key(seed), 6)
    route_ids_keys = jax.random.split(jax.random.fold_in(key_of[0], 1), TOKENS // TOK_DEV)
    route_ids_turns = jax.random.permutation(jax.random.fold_in(key_of[0], 3), TOKENS // TOK_DEV)
    route_ids = jax.vmap(lambda own, number: shared_out(jax.random.fold_in(key_of[0], 2), own, number, TOK_DEV, EXPERTS, TOP, CAP, 2))(route_ids_keys, route_ids_turns).reshape((TOKENS, TOP))
    gate_values = jnp.clip(jnp.exp(math.log(1.0) - 2.3025851 * jax.random.uniform(key_of[1], (TOKENS, TOP), jnp.float32) ** block_levels(key_of[1], (TOKENS, TOP), ((0, 1024),), -0.2, 0.2)), 0.1, 1.0)
    out_grad = bell_draw(key_of[2], (TOKENS, D_W), 0.25, 4.0, ((0, 1024),))
    down_weight = bell_draw(key_of[3], (EXPERTS, H, D_W), H ** -0.5, 0.21875, ((0, 32),))
    hidden = gaussian_with(key_of[4], (N_DP, EXPERTS, N_EXPERT, CAP, H), 1.0, 6.0, ((0, 32), (1, 32)), (0, 4, 32, 2.75))
    return dict(route_ids=route_ids, gate_values=gate_values, out_grad=out_grad, down_weight=down_weight, hidden=hidden)


def slot_table(route_ids, experts, capacity):
    flat_ids = route_ids.reshape(-1)
    route_count = flat_ids.shape[0]
    onehot = (flat_ids[:, None] == jnp.arange(experts, dtype=jnp.int32)[None, :]).astype(jnp.float32)
    positions = jnp.arange(route_count, dtype=jnp.int32)
    earlier = (positions[:, None] > positions[None, :]).astype(jnp.float32)
    before = jnp.dot(earlier, onehot, precision=lax.Precision.HIGHEST, preferred_element_type=jnp.float32)
    slot_rank = jnp.sum(before * onehot, axis=1).astype(jnp.int32)
    slot_index = flat_ids * capacity + slot_rank
    slots_all = jnp.arange(experts * capacity, dtype=jnp.int32)
    return (slots_all[:, None] == slot_index[None, :]).astype(jnp.float32)


def reference(route_ids, gate_values, out_grad, down_weight, hidden):
    ids_all = route_ids.reshape(N_DP, N_EXPERT, TOK_DEV, TOP)
    gates_all = gate_values.reshape(N_DP, N_EXPERT, TOK_DEV, TOP)
    grads_all = out_grad.reshape(N_DP, N_EXPERT, TOK_DEV, D_W)
    weight_f = down_weight.astype(jnp.float32)

    def one_source(ids_one, gates_one, grads_one, outs_one):
        slot_map = slot_table(ids_one, EXPERTS, CAP)
        rows_back = outs_one.reshape(EXPERTS * CAP, D_W).astype(jnp.float32)
        routed = jnp.dot(slot_map.T, rows_back, precision=lax.Precision.HIGHEST, preferred_element_type=jnp.float32)
        routed = routed.reshape(TOK_DEV, TOP, D_W)
        grads_f = grads_one.astype(jnp.float32)
        mixed_one = jnp.sum(gates_one[:, :, None] * routed, axis=1).astype(jnp.bfloat16)
        gate_one = jnp.sum(routed * grads_f[:, None, :], axis=2)
        scaled = (gates_one[:, :, None] * grads_f[:, None, :]).reshape(TOK_DEV * TOP, D_W).astype(jnp.bfloat16)
        outgoing = jnp.dot(slot_map, scaled.astype(jnp.float32), precision=lax.Precision.HIGHEST, preferred_element_type=jnp.float32)
        outgoing = outgoing.astype(jnp.bfloat16).reshape(EXPERTS, CAP, D_W)
        return mixed_one, gate_one, outgoing

    def per_group(total_grad, inputs):
        ids_grp, gates_grp, grads_grp, hidden_grp = inputs
        hidden_f = hidden_grp.astype(jnp.float32)
        expert_out = jnp.einsum("esch,ehd->escd", hidden_f, weight_f).astype(jnp.bfloat16)
        by_source = jnp.transpose(expert_out, (1, 0, 2, 3))
        mixed_grp, gate_grp, sent = jax.vmap(one_source)(ids_grp, gates_grp, grads_grp, by_source)
        expert_grad = jnp.transpose(sent, (1, 0, 2, 3)).astype(jnp.float32)
        hidden_grad = jnp.einsum("escd,ehd->esch", expert_grad, weight_f).astype(jnp.bfloat16)
        partial_term = jnp.einsum("esch,escd->ehd", hidden_f, expert_grad)
        return total_grad + partial_term, (mixed_grp, gate_grp, hidden_grad)

    start_grad = jnp.zeros((EXPERTS, H, D_W), jnp.float32)
    weight_grad, (mixed_all, gate_all, hidden_grad) = lax.scan(per_group, start_grad, (ids_all, gates_all, grads_all, hidden))
    return (mixed_all.reshape(TOKENS, D_W), gate_all.reshape(TOKENS, TOP), hidden_grad, weight_grad)
```

```python
import jax
import jax.numpy as jnp
from jax import lax
from jax.sharding import Mesh
from jax.sharding import PartitionSpec as P


def slot_table(route_ids, experts, capacity):
    flat_ids = route_ids.reshape(-1)
    route_count = flat_ids.shape[0]
    onehot = (flat_ids[:, None] == jnp.arange(experts, dtype=jnp.int32)[None, :]).astype(
        jnp.float32
    )
    positions = jnp.arange(route_count, dtype=jnp.int32)
    earlier = (positions[:, None] > positions[None, :]).astype(jnp.float32)
    before = jnp.dot(
        earlier, onehot, precision=lax.Precision.HIGHEST, preferred_element_type=jnp.float32
    )
    slot_rank = jnp.sum(before * onehot, axis=1).astype(jnp.int32)
    slot_index = flat_ids * capacity + slot_rank
    slots_all = jnp.arange(experts * capacity, dtype=jnp.int32)
    return (slots_all[:, None] == slot_index[None, :]).astype(jnp.bfloat16)


def on_device(route_ids, gate_values, out_grad, down_weight, hidden):
    experts = lax.axis_size("expert")
    chips = lax.axis_size("z")
    cores = lax.axis_size("core")
    capacity = hidden.shape[3]
    inner_width = hidden.shape[4]
    feature_width = out_grad.shape[1]
    tok_rows = route_ids.shape[0]
    routes = route_ids.shape[1]
    slot_map = slot_table(route_ids, experts, capacity)
    weight_mat = down_weight[0]
    rows_in = hidden.reshape(-1, inner_width)
    expert_out = jnp.dot(rows_in, weight_mat, preferred_element_type=jnp.float32)
    expert_out = expert_out.astype(jnp.bfloat16).reshape(experts, capacity, feature_width)
    grads_f = out_grad.astype(jnp.float32)
    scaled = (
        (gate_values[:, :, None] * grads_f[:, None, :])
        .reshape(-1, feature_width)
        .astype(jnp.bfloat16)
    )
    outgoing = jnp.dot(slot_map, scaled, preferred_element_type=jnp.float32)
    outgoing = outgoing.astype(jnp.bfloat16).reshape(experts, capacity, feature_width)
    incoming = lax.all_to_all(outgoing, "expert", split_axis=0, concat_axis=0, tiled=True)
    grad_rows = incoming.reshape(-1, feature_width)
    block = inner_width // (chips * cores)
    rows_perm = (
        rows_in.reshape(-1, chips, cores, block).transpose(0, 2, 1, 3).reshape(-1, inner_width)
    )
    partial_term = jnp.einsum(
        "sh,sd->hd", rows_perm, grad_rows, preferred_element_type=jnp.float32
    )
    half = lax.psum_scatter(partial_term, "core", scatter_dimension=0, tiled=True)
    weight_grad = lax.psum_scatter(half, "z", scatter_dimension=0, tiled=True)
    returned = lax.all_to_all(expert_out, "expert", split_axis=0, concat_axis=0, tiled=True)
    gathered = jnp.einsum(
        "sr,sd->rd",
        slot_map,
        returned.reshape(-1, feature_width),
        preferred_element_type=jnp.float32,
    )
    gathered = gathered.reshape(tok_rows, routes, feature_width)
    mixed_out = jnp.sum(gate_values[:, :, None] * gathered, axis=1).astype(jnp.bfloat16)
    gate_grad = jnp.sum(gathered * grads_f[:, None, :], axis=2)
    hidden_grad = jnp.einsum("sd,hd->sh", grad_rows, weight_mat, preferred_element_type=jnp.float32)
    hidden_grad = hidden_grad.astype(jnp.bfloat16).reshape(hidden.shape)
    return (mixed_out, gate_grad, hidden_grad, weight_grad[None])


def solution(mesh):
    n_dp = mesh.shape["dp"]
    n_ex = mesh.shape["expert"]
    sub = Mesh(mesh.devices.reshape(n_dp // 2, 2, n_ex), ("z", "core", "expert"))
    tok = ("z", "core", "expert")
    in_specs = (
        P(tok, None),
        P(tok, None),
        P(tok, None),
        P("expert", None, None),
        P(("z", "core"), "expert", None, None, None),
    )
    out_specs = (
        P(tok, None),
        P(tok, None),
        P(("z", "core"), "expert", None, None, None),
        P("expert", ("z", "core"), None),
    )
    return jax.shard_map(
        on_device, mesh=sub, in_specs=in_specs, out_specs=out_specs, check_vma=False
    )
```

```python
import jax
import jax.numpy as jnp
from jax import lax
from jax.sharding import Mesh
from jax.sharding import PartitionSpec as P


def slot_table(route_ids, experts, capacity):
    flat_ids = route_ids.reshape(-1)
    route_count = flat_ids.shape[0]
    onehot = (flat_ids[:, None] == jnp.arange(experts, dtype=jnp.int32)[None, :]).astype(
        jnp.float32
    )
    positions = jnp.arange(route_count, dtype=jnp.int32)
    earlier = (positions[:, None] > positions[None, :]).astype(jnp.float32)
    before = jnp.dot(
        earlier, onehot, precision=lax.Precision.HIGHEST, preferred_element_type=jnp.float32
    )
    slot_rank = jnp.sum(before * onehot, axis=1).astype(jnp.int32)
    slot_index = flat_ids * capacity + slot_rank
    slots_all = jnp.arange(experts * capacity, dtype=jnp.int32)
    return (slots_all[:, None] == slot_index[None, :]).astype(jnp.bfloat16)


def ring_reduce_scatter(blocks, axis, n):
    d = lax.axis_index(axis)
    down = [(i, (i - 1) % n) for i in range(n)]
    up = [(i, (i + 1) % n) for i in range(n)]

    def blk(j):
        return lax.dynamic_index_in_dim(blocks, j % n, axis=0, keepdims=False)

    n_a = n // 2
    n_b = n - 1 - n_a
    acc_a = None
    acc_b = None
    for t in range(n_a):
        own = blk(d + n - n_a + t)
        acc_a = lax.ppermute(own if acc_a is None else acc_a + own, axis, down)
        if t < n_b:
            own_b = blk(d + n_b - t)
            acc_b = lax.ppermute(own_b if acc_b is None else acc_b + own_b, axis, up)
    out = blk(d) + acc_a
    if acc_b is not None:
        out = out + acc_b
    return out


def reduce_over_dp(partial_term, chips, cores):
    rows = partial_term.shape[0]
    parts = partial_term.reshape(cores, chips, rows // (cores * chips), -1)
    c = lax.axis_index("core")
    keep = lax.dynamic_index_in_dim(parts, c, axis=0, keepdims=False)
    give = lax.dynamic_index_in_dim(parts, 1 - c, axis=0, keepdims=False)
    got = lax.ppermute(give, "core", [(0, 1), (1, 0)])
    return ring_reduce_scatter(keep + got, "z", chips)


def on_device(route_ids, gate_values, out_grad, down_weight, hidden):
    experts = lax.axis_size("expert")
    chips = lax.axis_size("z")
    cores = lax.axis_size("core")
    capacity = hidden.shape[3]
    inner_width = hidden.shape[4]
    feature_width = out_grad.shape[1]
    tok_rows = route_ids.shape[0]
    routes = route_ids.shape[1]
    slot_map = slot_table(route_ids, experts, capacity)
    weight_mat = down_weight[0]
    rows_in = hidden.reshape(-1, inner_width)
    expert_out = jnp.dot(rows_in, weight_mat, preferred_element_type=jnp.float32)
    expert_out = expert_out.astype(jnp.bfloat16).reshape(experts, capacity, feature_width)
    grads_f = out_grad.astype(jnp.float32)
    scaled = (
        (gate_values[:, :, None] * grads_f[:, None, :])
        .reshape(-1, feature_width)
        .astype(jnp.bfloat16)
    )
    outgoing = jnp.dot(slot_map, scaled, preferred_element_type=jnp.float32)
    outgoing = outgoing.astype(jnp.bfloat16).reshape(experts, capacity, feature_width)
    incoming = lax.all_to_all(outgoing, "expert", split_axis=0, concat_axis=0, tiled=True)
    grad_rows = incoming.reshape(-1, feature_width)
    block = inner_width // (chips * cores)
    rows_perm = (
        rows_in.reshape(-1, chips, cores, block).transpose(0, 2, 1, 3).reshape(-1, inner_width)
    )
    partial_term = jnp.einsum(
        "sh,sd->hd", rows_perm, grad_rows, preferred_element_type=jnp.float32
    )
    weight_grad = reduce_over_dp(partial_term, chips, cores)
    returned = lax.all_to_all(expert_out, "expert", split_axis=0, concat_axis=0, tiled=True)
    gathered = jnp.einsum(
        "sr,sd->rd",
        slot_map,
        returned.reshape(-1, feature_width),
        preferred_element_type=jnp.float32,
    )
    gathered = gathered.reshape(tok_rows, routes, feature_width)
    mixed_out = jnp.sum(gate_values[:, :, None] * gathered, axis=1).astype(jnp.bfloat16)
    gate_grad = jnp.sum(gathered * grads_f[:, None, :], axis=2)
    hidden_grad = jnp.einsum("sd,hd->sh", grad_rows, weight_mat, preferred_element_type=jnp.float32)
    hidden_grad = hidden_grad.astype(jnp.bfloat16).reshape(hidden.shape)
    return (mixed_out, gate_grad, hidden_grad, weight_grad[None])


def solution(mesh):
    n_dp = mesh.shape["dp"]
    n_ex = mesh.shape["expert"]
    sub = Mesh(mesh.devices.reshape(n_dp // 2, 2, n_ex), ("z", "core", "expert"))
    tok = ("z", "core", "expert")
    in_specs = (
        P(tok, None),
        P(tok, None),
        P(tok, None),
        P("expert", None, None),
        P(("z", "core"), "expert", None, None, None),
    )
    out_specs = (
        P(tok, None),
        P(tok, None),
        P(("z", "core"), "expert", None, None, None),
        P("expert", ("z", "core"), None),
    )
    return jax.shard_map(
        on_device, mesh=sub, in_specs=in_specs, out_specs=out_specs, check_vma=False
    )
```

```python
import jax
import jax.numpy as jnp
from jax import lax
from jax.sharding import Mesh
from jax.sharding import PartitionSpec as P


def slot_table(route_ids, experts, capacity):
    flat_ids = route_ids.reshape(-1)
    route_count = flat_ids.shape[0]
    onehot = (flat_ids[:, None] == jnp.arange(experts, dtype=jnp.int32)[None, :]).astype(
        jnp.float32
    )
    positions = jnp.arange(route_count, dtype=jnp.int32)
    earlier = (positions[:, None] > positions[None, :]).astype(jnp.float32)
    before = jnp.dot(
        earlier, onehot, precision=lax.Precision.HIGHEST, preferred_element_type=jnp.float32
    )
    slot_rank = jnp.sum(before * onehot, axis=1).astype(jnp.int32)
    slot_index = flat_ids * capacity + slot_rank
    slots_all = jnp.arange(experts * capacity, dtype=jnp.int32)
    return (slots_all[:, None] == slot_index[None, :]).astype(jnp.bfloat16)


def reduce_over_dp(partial_term, chips, cores):
    rows = partial_term.shape[0]
    parts = partial_term.reshape(cores, chips, rows // (cores * chips), -1)
    c = lax.axis_index("core")
    keep = lax.dynamic_index_in_dim(parts, c, axis=0, keepdims=False)
    give = lax.dynamic_index_in_dim(parts, 1 - c, axis=0, keepdims=False)
    got = lax.ppermute(give, "core", [(0, 1), (1, 0)])
    chip_sum = (keep + got).reshape(rows // cores, -1)
    return lax.psum_scatter(chip_sum, "z", scatter_dimension=0, tiled=True)


def on_device(route_ids, gate_values, out_grad, down_weight, hidden):
    experts = lax.axis_size("expert")
    chips = lax.axis_size("z")
    cores = lax.axis_size("core")
    capacity = hidden.shape[3]
    inner_width = hidden.shape[4]
    feature_width = out_grad.shape[1]
    tok_rows = route_ids.shape[0]
    routes = route_ids.shape[1]
    slot_map = slot_table(route_ids, experts, capacity)
    weight_mat = down_weight[0]
    rows_in = hidden.reshape(-1, inner_width)
    expert_out = jnp.dot(rows_in, weight_mat, preferred_element_type=jnp.float32)
    expert_out = expert_out.astype(jnp.bfloat16).reshape(experts, capacity, feature_width)
    grads_f = out_grad.astype(jnp.float32)
    scaled = (
        (gate_values[:, :, None] * grads_f[:, None, :])
        .reshape(-1, feature_width)
        .astype(jnp.bfloat16)
    )
    outgoing = jnp.dot(slot_map, scaled, preferred_element_type=jnp.float32)
    outgoing = outgoing.astype(jnp.bfloat16).reshape(experts, capacity, feature_width)
    incoming = lax.all_to_all(outgoing, "expert", split_axis=0, concat_axis=0, tiled=True)
    grad_rows = incoming.reshape(-1, feature_width)
    block = inner_width // (chips * cores)
    rows_perm = (
        rows_in.reshape(-1, chips, cores, block).transpose(0, 2, 1, 3).reshape(-1, inner_width)
    )
    partial_term = jnp.einsum(
        "sh,sd->hd", rows_perm, grad_rows, preferred_element_type=jnp.float32
    )
    weight_grad = reduce_over_dp(partial_term, chips, cores)
    returned = lax.all_to_all(expert_out, "expert", split_axis=0, concat_axis=0, tiled=True)
    gathered = jnp.einsum(
        "sr,sd->rd",
        slot_map,
        returned.reshape(-1, feature_width),
        preferred_element_type=jnp.float32,
    )
    gathered = gathered.reshape(tok_rows, routes, feature_width)
    mixed_out = jnp.sum(gate_values[:, :, None] * gathered, axis=1).astype(jnp.bfloat16)
    gate_grad = jnp.sum(gathered * grads_f[:, None, :], axis=2)
    hidden_grad = jnp.einsum("sd,hd->sh", grad_rows, weight_mat, preferred_element_type=jnp.float32)
    hidden_grad = hidden_grad.astype(jnp.bfloat16).reshape(hidden.shape)
    return (mixed_out, gate_grad, hidden_grad, weight_grad[None])


def solution(mesh):
    n_dp = mesh.shape["dp"]
    n_ex = mesh.shape["expert"]
    sub = Mesh(mesh.devices.reshape(n_dp // 2, 2, n_ex), ("z", "core", "expert"))
    tok = ("z", "core", "expert")
    in_specs = (
        P(tok, None),
        P(tok, None),
        P(tok, None),
        P("expert", None, None),
        P(("z", "core"), "expert", None, None, None),
    )
    out_specs = (
        P(tok, None),
        P(tok, None),
        P(("z", "core"), "expert", None, None, None),
        P("expert", ("z", "core"), None),
    )
    return jax.shard_map(
        on_device, mesh=sub, in_specs=in_specs, out_specs=out_specs, check_vma=False
    )
```

```python
import jax
import jax.numpy as jnp
from jax import lax
from jax.sharding import Mesh
from jax.sharding import PartitionSpec as P


def slot_table(route_ids, experts, capacity):
    flat_ids = route_ids.reshape(-1)
    route_count = flat_ids.shape[0]
    onehot = (flat_ids[:, None] == jnp.arange(experts, dtype=jnp.int32)[None, :]).astype(
        jnp.float32
    )
    positions = jnp.arange(route_count, dtype=jnp.int32)
    earlier = (positions[:, None] > positions[None, :]).astype(jnp.float32)
    before = jnp.dot(
        earlier, onehot, precision=lax.Precision.HIGHEST, preferred_element_type=jnp.float32
    )
    slot_rank = jnp.sum(before * onehot, axis=1).astype(jnp.int32)
    slot_index = flat_ids * capacity + slot_rank
    slots_all = jnp.arange(experts * capacity, dtype=jnp.int32)
    return (slots_all[:, None] == slot_index[None, :]).astype(jnp.bfloat16)


def on_device(route_ids, gate_values, out_grad, down_weight, hidden):
    experts = lax.axis_size("expert")
    chips = lax.axis_size("z")
    cores = lax.axis_size("core")
    capacity = hidden.shape[3]
    inner_width = hidden.shape[4]
    feature_width = out_grad.shape[1]
    tok_rows = route_ids.shape[0]
    routes = route_ids.shape[1]
    slot_map = slot_table(route_ids, experts, capacity)
    weight_mat = down_weight[0]
    rows_in = hidden.reshape(-1, inner_width)
    expert_out = jnp.dot(rows_in, weight_mat, preferred_element_type=jnp.float32)
    expert_out = expert_out.astype(jnp.bfloat16).reshape(experts, capacity, feature_width)
    grads_f = out_grad.astype(jnp.float32)
    scaled = (
        (gate_values[:, :, None] * grads_f[:, None, :])
        .reshape(-1, feature_width)
        .astype(jnp.bfloat16)
    )
    outgoing = jnp.dot(slot_map, scaled, preferred_element_type=jnp.float32)
    outgoing = outgoing.astype(jnp.bfloat16).reshape(experts, capacity, feature_width)
    block = inner_width // (chips * cores)
    c = lax.axis_index("core")
    swap = [(0, 1), (1, 0)]
    cols = rows_in.reshape(-1, chips, cores, block)
    mine_cols = lax.dynamic_index_in_dim(cols, c, axis=2, keepdims=False)
    give_cols = lax.dynamic_index_in_dim(cols, 1 - c, axis=2, keepdims=False)
    got_cols = lax.ppermute(give_cols, "core", swap)
    both_cols = jnp.concatenate([mine_cols, got_cols], axis=0).reshape(-1, chips * block)
    n_split = 2
    width = feature_width // n_split
    grad_parts = []
    weight_parts = []
    for k in range(n_split):
        piece = outgoing[:, :, k * width : (k + 1) * width]
        got = lax.all_to_all(piece, "expert", split_axis=0, concat_axis=0, tiled=True)
        got = got.reshape(-1, width)
        grad_parts.append(got)
        partner = lax.ppermute(got, "core", swap)
        both = jnp.concatenate([got, partner], axis=0)
        chip_part = jnp.einsum("sh,sd->hd", both_cols, both, preferred_element_type=jnp.float32)
        weight_parts.append(lax.psum_scatter(chip_part, "z", scatter_dimension=0, tiled=True))
    weight_grad = jnp.concatenate(weight_parts, axis=1)
    grad_rows = jnp.concatenate(grad_parts, axis=1)
    returned = lax.all_to_all(expert_out, "expert", split_axis=0, concat_axis=0, tiled=True)
    gathered = jnp.einsum(
        "sr,sd->rd",
        slot_map,
        returned.reshape(-1, feature_width),
        preferred_element_type=jnp.float32,
    )
    gathered = gathered.reshape(tok_rows, routes, feature_width)
    mixed_out = jnp.sum(gate_values[:, :, None] * gathered, axis=1).astype(jnp.bfloat16)
    gate_grad = jnp.sum(gathered * grads_f[:, None, :], axis=2)
    hidden_grad = jnp.einsum("sd,hd->sh", grad_rows, weight_mat, preferred_element_type=jnp.float32)
    hidden_grad = hidden_grad.astype(jnp.bfloat16).reshape(hidden.shape)
    return (mixed_out, gate_grad, hidden_grad, weight_grad[None])


def solution(mesh):
    n_dp = mesh.shape["dp"]
    n_ex = mesh.shape["expert"]
    sub = Mesh(mesh.devices.reshape(n_dp // 2, 2, n_ex), ("z", "core", "expert"))
    tok = ("z", "core", "expert")
    in_specs = (
        P(tok, None),
        P(tok, None),
        P(tok, None),
        P("expert", None, None),
        P(("z", "core"), "expert", None, None, None),
    )
    out_specs = (
        P(tok, None),
        P(tok, None),
        P(("z", "core"), "expert", None, None, None),
        P("expert", ("z", "core"), None),
    )
    return jax.shard_map(
        on_device, mesh=sub, in_specs=in_specs, out_specs=out_specs, check_vma=False
    )
```

```python
import jax
import jax.numpy as jnp
from jax import lax
from jax.sharding import Mesh
from jax.sharding import PartitionSpec as P


def slot_table(route_ids, experts, capacity):
    flat_ids = route_ids.reshape(-1)
    route_count = flat_ids.shape[0]
    onehot = (flat_ids[:, None] == jnp.arange(experts, dtype=jnp.int32)[None, :]).astype(
        jnp.float32
    )
    positions = jnp.arange(route_count, dtype=jnp.int32)
    earlier = (positions[:, None] > positions[None, :]).astype(jnp.float32)
    before = jnp.dot(
        earlier, onehot, precision=lax.Precision.HIGHEST, preferred_element_type=jnp.float32
    )
    slot_rank = jnp.sum(before * onehot, axis=1).astype(jnp.int32)
    slot_index = flat_ids * capacity + slot_rank
    slots_all = jnp.arange(experts * capacity, dtype=jnp.int32)
    return (slots_all[:, None] == slot_index[None, :]).astype(jnp.bfloat16)


def reduce_over_dp(partial_term, chips, cores):
    rows = partial_term.shape[0]
    parts = partial_term.reshape(cores, chips, rows // (cores * chips), -1)
    c = lax.axis_index("core")
    keep = lax.dynamic_index_in_dim(parts, c, axis=0, keepdims=False)
    give = lax.dynamic_index_in_dim(parts, 1 - c, axis=0, keepdims=False)
    got = lax.ppermute(give, "core", [(0, 1), (1, 0)])
    chip_sum = (keep + got).reshape(rows // cores, -1)
    near = lax.psum_scatter(chip_sum, "z_lo", scatter_dimension=0, tiled=True)
    return lax.psum_scatter(near, "z_hi", scatter_dimension=0, tiled=True)


def on_device(route_ids, gate_values, out_grad, down_weight, hidden):
    experts = lax.axis_size("expert")
    z_hi = lax.axis_size("z_hi")
    z_lo = lax.axis_size("z_lo")
    chips = z_hi * z_lo
    cores = lax.axis_size("core")
    capacity = hidden.shape[3]
    inner_width = hidden.shape[4]
    feature_width = out_grad.shape[1]
    tok_rows = route_ids.shape[0]
    routes = route_ids.shape[1]
    slot_map = slot_table(route_ids, experts, capacity)
    weight_mat = down_weight[0]
    rows_in = hidden.reshape(-1, inner_width)
    expert_out = jnp.dot(rows_in, weight_mat, preferred_element_type=jnp.float32)
    expert_out = expert_out.astype(jnp.bfloat16).reshape(experts, capacity, feature_width)
    grads_f = out_grad.astype(jnp.float32)
    scaled = (
        (gate_values[:, :, None] * grads_f[:, None, :])
        .reshape(-1, feature_width)
        .astype(jnp.bfloat16)
    )
    outgoing = jnp.dot(slot_map, scaled, preferred_element_type=jnp.float32)
    outgoing = outgoing.astype(jnp.bfloat16).reshape(experts, capacity, feature_width)
    incoming = lax.all_to_all(outgoing, "expert", split_axis=0, concat_axis=0, tiled=True)
    grad_rows = incoming.reshape(-1, feature_width)
    block = inner_width // (chips * cores)
    rows_perm = (
        rows_in.reshape(-1, z_hi, z_lo, cores, block)
        .transpose(0, 3, 2, 1, 4)
        .reshape(-1, inner_width)
    )
    partial_term = jnp.einsum(
        "sh,sd->hd", rows_perm, grad_rows, preferred_element_type=jnp.float32
    )
    weight_grad = reduce_over_dp(partial_term, chips, cores)
    returned = lax.all_to_all(expert_out, "expert", split_axis=0, concat_axis=0, tiled=True)
    gathered = jnp.einsum(
        "sr,sd->rd",
        slot_map,
        returned.reshape(-1, feature_width),
        preferred_element_type=jnp.float32,
    )
    gathered = gathered.reshape(tok_rows, routes, feature_width)
    mixed_out = jnp.sum(gate_values[:, :, None] * gathered, axis=1).astype(jnp.bfloat16)
    gate_grad = jnp.sum(gathered * grads_f[:, None, :], axis=2)
    hidden_grad = jnp.einsum("sd,hd->sh", grad_rows, weight_mat, preferred_element_type=jnp.float32)
    hidden_grad = hidden_grad.astype(jnp.bfloat16).reshape(hidden.shape)
    return (mixed_out, gate_grad, hidden_grad, weight_grad[None])


def solution(mesh):
    n_dp = mesh.shape["dp"]
    n_ex = mesh.shape["expert"]
    n_lo = 4 if n_dp % 8 == 0 else 1
    sub = Mesh(
        mesh.devices.reshape(n_dp // (2 * n_lo), n_lo, 2, n_ex), ("z_hi", "z_lo", "core", "expert")
    )
    dp = ("z_hi", "z_lo", "core")
    tok = dp + ("expert",)
    in_specs = (
        P(tok, None),
        P(tok, None),
        P(tok, None),
        P("expert", None, None),
        P(dp, "expert", None, None, None),
    )
    out_specs = (
        P(tok, None),
        P(tok, None),
        P(dp, "expert", None, None, None),
        P("expert", dp, None),
    )
    return jax.shard_map(
        on_device, mesh=sub, in_specs=in_specs, out_specs=out_specs, check_vma=False
    )
```

```python
import jax
import jax.numpy as jnp
from jax import lax
from jax.sharding import Mesh
from jax.sharding import PartitionSpec as P


def slot_table(route_ids, experts, capacity):
    flat_ids = route_ids.reshape(-1)
    route_count = flat_ids.shape[0]
    onehot = (flat_ids[:, None] == jnp.arange(experts, dtype=jnp.int32)[None, :]).astype(
        jnp.float32
    )
    positions = jnp.arange(route_count, dtype=jnp.int32)
    earlier = (positions[:, None] > positions[None, :]).astype(jnp.float32)
    before = jnp.dot(
        earlier, onehot, precision=lax.Precision.HIGHEST, preferred_element_type=jnp.float32
    )
    slot_rank = jnp.sum(before * onehot, axis=1).astype(jnp.int32)
    slot_index = flat_ids * capacity + slot_rank
    slots_all = jnp.arange(experts * capacity, dtype=jnp.int32)
    return (slots_all[:, None] == slot_index[None, :]).astype(jnp.bfloat16)


def on_device(route_ids, gate_values, out_grad, down_weight, hidden):
    experts = lax.axis_size("expert")
    chips = lax.axis_size("z")
    cores = lax.axis_size("core")
    capacity = hidden.shape[3]
    inner_width = hidden.shape[4]
    feature_width = out_grad.shape[1]
    tok_rows = route_ids.shape[0]
    routes = route_ids.shape[1]
    slot_map = slot_table(route_ids, experts, capacity)
    weight_mat = down_weight[0]
    rows_in = hidden.reshape(-1, inner_width)
    expert_out = jnp.dot(rows_in, weight_mat, preferred_element_type=jnp.float32)
    expert_out = expert_out.astype(jnp.bfloat16).reshape(experts, capacity, feature_width)
    grads_f = out_grad.astype(jnp.float32)
    by_token = slot_map.reshape(-1, tok_rows, routes)
    token_hot = jnp.sum(by_token, axis=2)
    slot_gate = jnp.sum(by_token.astype(jnp.float32) * gate_values[None], axis=(1, 2))
    slot_grads = jnp.dot(token_hot, out_grad, preferred_element_type=jnp.float32)
    outgoing = (slot_gate[:, None] * slot_grads).astype(jnp.bfloat16)
    outgoing = outgoing.reshape(experts, capacity, feature_width)
    incoming = lax.all_to_all(outgoing, "expert", split_axis=0, concat_axis=0, tiled=True)
    grad_rows = incoming.reshape(-1, feature_width)
    block = inner_width // (chips * cores)
    c = lax.axis_index("core")
    swap = [(0, 1), (1, 0)]
    col_of = jnp.arange(inner_width, dtype=jnp.int32).reshape(chips, cores, block)

    def columns(core):
        pick = col_of[:, 0, :].reshape(-1) + core * block
        sel = (jnp.arange(inner_width, dtype=jnp.int32)[:, None] == pick[None, :])
        return jnp.dot(rows_in, sel.astype(jnp.bfloat16), preferred_element_type=jnp.float32)

    mine_cols = columns(c).astype(jnp.bfloat16)
    got_cols = lax.ppermute(columns(1 - c).astype(jnp.bfloat16), "core", swap)
    both_cols = jnp.concatenate([mine_cols, got_cols], axis=0)
    partner = lax.ppermute(grad_rows, "core", swap)
    both = jnp.concatenate([grad_rows, partner], axis=0)
    chip_part = jnp.einsum("sh,sd->hd", both_cols, both, preferred_element_type=jnp.float32)
    weight_grad = lax.psum_scatter(chip_part, "z", scatter_dimension=0, tiled=True)
    returned = lax.all_to_all(expert_out, "expert", split_axis=0, concat_axis=0, tiled=True)
    gathered = jnp.einsum(
        "sr,sd->rd",
        slot_map,
        returned.reshape(-1, feature_width),
        preferred_element_type=jnp.float32,
    )
    gathered = gathered.reshape(tok_rows, routes, feature_width)
    mixed_out = jnp.sum(gate_values[:, :, None] * gathered, axis=1).astype(jnp.bfloat16)
    gate_grad = jnp.sum(gathered * grads_f[:, None, :], axis=2)
    hidden_grad = jnp.einsum("sd,hd->sh", grad_rows, weight_mat, preferred_element_type=jnp.float32)
    hidden_grad = hidden_grad.astype(jnp.bfloat16).reshape(hidden.shape)
    return (mixed_out, gate_grad, hidden_grad, weight_grad[None])


def solution(mesh):
    n_dp = mesh.shape["dp"]
    n_ex = mesh.shape["expert"]
    sub = Mesh(mesh.devices.reshape(n_dp // 2, 2, n_ex), ("z", "core", "expert"))
    tok = ("z", "core", "expert")
    in_specs = (
        P(tok, None),
        P(tok, None),
        P(tok, None),
        P("expert", None, None),
        P(("z", "core"), "expert", None, None, None),
    )
    out_specs = (
        P(tok, None),
        P(tok, None),
        P(("z", "core"), "expert", None, None, None),
        P("expert", ("z", "core"), None),
    )
    return jax.shard_map(
        on_device, mesh=sub, in_specs=in_specs, out_specs=out_specs, check_vma=False
    )
```

```python
import jax
import jax.numpy as jnp
from jax import lax
from jax.sharding import Mesh
from jax.sharding import PartitionSpec as P


def slot_table(route_ids, experts, capacity):
    flat_ids = route_ids.reshape(-1)
    route_count = flat_ids.shape[0]
    onehot = (flat_ids[:, None] == jnp.arange(experts, dtype=jnp.int32)[None, :]).astype(
        jnp.float32
    )
    positions = jnp.arange(route_count, dtype=jnp.int32)
    earlier = (positions[:, None] > positions[None, :]).astype(jnp.float32)
    before = jnp.dot(
        earlier, onehot, precision=lax.Precision.HIGHEST, preferred_element_type=jnp.float32
    )
    slot_rank = jnp.sum(before * onehot, axis=1).astype(jnp.int32)
    slot_index = flat_ids * capacity + slot_rank
    slots_all = jnp.arange(experts * capacity, dtype=jnp.int32)
    return (slots_all[:, None] == slot_index[None, :]).astype(jnp.bfloat16)


def on_device(route_ids, gate_values, out_grad, down_weight, hidden):
    experts = lax.axis_size("expert")
    chips = lax.axis_size("z")
    cores = lax.axis_size("core")
    capacity = hidden.shape[3]
    inner_width = hidden.shape[4]
    feature_width = out_grad.shape[1]
    tok_rows = route_ids.shape[0]
    routes = route_ids.shape[1]
    slot_map = slot_table(route_ids, experts, capacity)
    weight_mat = down_weight[0]
    rows_in = hidden[0, 0]
    expert_out = jnp.einsum("sch,hd->scd", rows_in, weight_mat, preferred_element_type=jnp.float32)
    expert_out = expert_out.astype(jnp.bfloat16)
    grads_f = out_grad.astype(jnp.float32)
    by_token = slot_map.reshape(experts, capacity, tok_rows, routes)
    token_hot = jnp.sum(by_token, axis=3)
    slot_gate = jnp.sum(by_token.astype(jnp.float32) * gate_values[None, None], axis=(2, 3))
    slot_grads = jnp.einsum("ect,td->ecd", token_hot, out_grad, preferred_element_type=jnp.float32)
    outgoing = (slot_gate[:, :, None] * slot_grads).astype(jnp.bfloat16)
    grad_rows = lax.all_to_all(outgoing, "expert", split_axis=0, concat_axis=0, tiled=True)
    block = inner_width // (chips * cores)
    c = lax.axis_index("core")
    swap = [(0, 1), (1, 0)]
    col_of = jnp.arange(inner_width, dtype=jnp.int32).reshape(chips, cores, block)

    def columns(core):
        pick = col_of[:, 0, :].reshape(-1) + core * block
        sel = (jnp.arange(inner_width, dtype=jnp.int32)[:, None] == pick[None, :])
        return jnp.einsum(
            "sch,hj->scj", rows_in, sel.astype(jnp.bfloat16), preferred_element_type=jnp.float32
        )

    mine_cols = columns(c).astype(jnp.bfloat16)
    got_cols = lax.ppermute(columns(1 - c).astype(jnp.bfloat16), "core", swap)
    both_cols = jnp.concatenate([mine_cols, got_cols], axis=0)
    partner = lax.ppermute(grad_rows, "core", swap)
    both = jnp.concatenate([grad_rows, partner], axis=0)
    chip_part = jnp.einsum("sch,scd->hd", both_cols, both, preferred_element_type=jnp.float32)
    weight_grad = lax.psum_scatter(chip_part, "z", scatter_dimension=0, tiled=True)
    returned = lax.all_to_all(expert_out, "expert", split_axis=0, concat_axis=0, tiled=True)
    gathered = jnp.einsum(
        "ecr,ecd->rd",
        slot_map.reshape(experts, capacity, -1),
        returned,
        preferred_element_type=jnp.float32,
    )
    gathered = gathered.reshape(tok_rows, routes, feature_width)
    mixed_out = jnp.sum(gate_values[:, :, None] * gathered, axis=1).astype(jnp.bfloat16)
    gate_grad = jnp.sum(gathered * grads_f[:, None, :], axis=2)
    hidden_grad = jnp.einsum(
        "scd,hd->sch", grad_rows, weight_mat, preferred_element_type=jnp.float32
    )
    hidden_grad = hidden_grad.astype(jnp.bfloat16).reshape(hidden.shape)
    return (mixed_out, gate_grad, hidden_grad, weight_grad[None])


def solution(mesh):
    n_dp = mesh.shape["dp"]
    n_ex = mesh.shape["expert"]
    sub = Mesh(mesh.devices.reshape(n_dp // 2, 2, n_ex), ("z", "core", "expert"))
    tok = ("z", "core", "expert")
    in_specs = (
        P(tok, None),
        P(tok, None),
        P(tok, None),
        P("expert", None, None),
        P(("z", "core"), "expert", None, None, None),
    )
    out_specs = (
        P(tok, None),
        P(tok, None),
        P(("z", "core"), "expert", None, None, None),
        P("expert", ("z", "core"), None),
    )
    return jax.shard_map(
        on_device, mesh=sub, in_specs=in_specs, out_specs=out_specs, check_vma=False
    )
```

```python
import jax
import jax.numpy as jnp
from jax import lax
from jax.sharding import Mesh
from jax.sharding import PartitionSpec as P


def slot_table(route_ids, experts, capacity):
    flat_ids = route_ids.reshape(-1)
    route_count = flat_ids.shape[0]
    onehot = (flat_ids[:, None] == jnp.arange(experts, dtype=jnp.int32)[None, :]).astype(
        jnp.float32
    )
    positions = jnp.arange(route_count, dtype=jnp.int32)
    earlier = (positions[:, None] > positions[None, :]).astype(jnp.float32)
    before = jnp.dot(
        earlier, onehot, precision=lax.Precision.HIGHEST, preferred_element_type=jnp.float32
    )
    slot_rank = jnp.sum(before * onehot, axis=1).astype(jnp.int32)
    slot_index = flat_ids * capacity + slot_rank
    slots_all = jnp.arange(experts * capacity, dtype=jnp.int32)
    return (slots_all[:, None] == slot_index[None, :]).astype(jnp.bfloat16)


def on_device(route_ids, gate_values, out_grad, down_weight, hidden):
    experts = lax.axis_size("expert")
    chips = lax.axis_size("z")
    cores = lax.axis_size("core")
    capacity = hidden.shape[3]
    inner_width = hidden.shape[4]
    feature_width = out_grad.shape[1]
    tok_rows = route_ids.shape[0]
    routes = route_ids.shape[1]
    slot_map = slot_table(route_ids, experts, capacity)
    weight_mat = down_weight[0]
    rows_in = hidden[0, 0]
    expert_out = jnp.einsum("sch,hd->scd", rows_in, weight_mat, preferred_element_type=jnp.float32)
    expert_out = expert_out.astype(jnp.bfloat16)
    grads_f = out_grad.astype(jnp.float32)
    by_token = slot_map.reshape(experts, capacity, tok_rows, routes)
    token_hot = jnp.sum(by_token, axis=3)
    slot_gate = jnp.sum(by_token.astype(jnp.float32) * gate_values[None, None], axis=(2, 3))
    slot_grads = jnp.einsum("ect,td->ecd", token_hot, out_grad, preferred_element_type=jnp.float32)
    outgoing = (slot_gate[:, :, None] * slot_grads).astype(jnp.bfloat16)
    grad_rows = lax.all_to_all(outgoing, "expert", split_axis=0, concat_axis=0, tiled=True)
    block = inner_width // (chips * cores)
    c = lax.axis_index("core")
    swap = [(0, 1), (1, 0)]
    col_of = jnp.arange(inner_width, dtype=jnp.int32).reshape(chips, cores, block)

    def columns(core):
        pick = col_of[:, 0, :].reshape(-1) + core * block
        sel = (jnp.arange(inner_width, dtype=jnp.int32)[:, None] == pick[None, :])
        return jnp.einsum(
            "sch,hj->scj", rows_in, sel.astype(jnp.bfloat16), preferred_element_type=jnp.float32
        )

    mine_cols = columns(c).astype(jnp.bfloat16)
    got_cols = lax.ppermute(columns(1 - c).astype(jnp.bfloat16), "core", swap)
    both_cols = jnp.concatenate([mine_cols, got_cols], axis=0)
    partner = lax.ppermute(grad_rows, "core", swap)
    both = jnp.concatenate([grad_rows, partner], axis=0)
    chip_part = jnp.einsum("sch,scd->hd", both_cols, both, preferred_element_type=jnp.float32)
    chip_total = lax.psum(chip_part, "z")
    weight_grad = lax.dynamic_slice_in_dim(chip_total, lax.axis_index("z") * block, block, axis=0)
    returned = lax.all_to_all(expert_out, "expert", split_axis=0, concat_axis=0, tiled=True)
    gathered = jnp.einsum(
        "ecr,ecd->rd",
        slot_map.reshape(experts, capacity, -1),
        returned,
        preferred_element_type=jnp.float32,
    )
    gathered = gathered.reshape(tok_rows, routes, feature_width)
    mixed_out = jnp.sum(gate_values[:, :, None] * gathered, axis=1).astype(jnp.bfloat16)
    gate_grad = jnp.sum(gathered * grads_f[:, None, :], axis=2)
    hidden_grad = jnp.einsum(
        "scd,hd->sch", grad_rows, weight_mat, preferred_element_type=jnp.float32
    )
    hidden_grad = hidden_grad.astype(jnp.bfloat16).reshape(hidden.shape)
    return (mixed_out, gate_grad, hidden_grad, weight_grad[None])


def solution(mesh):
    n_dp = mesh.shape["dp"]
    n_ex = mesh.shape["expert"]
    sub = Mesh(mesh.devices.reshape(n_dp // 2, 2, n_ex), ("z", "core", "expert"))
    tok = ("z", "core", "expert")
    in_specs = (
        P(tok, None),
        P(tok, None),
        P(tok, None),
        P("expert", None, None),
        P(("z", "core"), "expert", None, None, None),
    )
    out_specs = (
        P(tok, None),
        P(tok, None),
        P(("z", "core"), "expert", None, None, None),
        P("expert", ("z", "core"), None),
    )
    return jax.shard_map(
        on_device, mesh=sub, in_specs=in_specs, out_specs=out_specs, check_vma=False
    )
```

```python
import jax
import jax.numpy as jnp
from jax import lax
from jax.sharding import Mesh
from jax.sharding import PartitionSpec as P


def slot_table(route_ids, experts, capacity):
    flat_ids = route_ids.reshape(-1)
    route_count = flat_ids.shape[0]
    onehot = (flat_ids[:, None] == jnp.arange(experts, dtype=jnp.int32)[None, :]).astype(
        jnp.float32
    )
    positions = jnp.arange(route_count, dtype=jnp.int32)
    earlier = (positions[:, None] > positions[None, :]).astype(jnp.float32)
    before = jnp.dot(
        earlier, onehot, precision=lax.Precision.HIGHEST, preferred_element_type=jnp.float32
    )
    slot_rank = jnp.sum(before * onehot, axis=1).astype(jnp.int32)
    slot_index = flat_ids * capacity + slot_rank
    slots_all = jnp.arange(experts * capacity, dtype=jnp.int32)
    return (slots_all[:, None] == slot_index[None, :]).astype(jnp.bfloat16)


def on_device(route_ids, gate_values, out_grad, down_weight, hidden):
    experts = lax.axis_size("expert")
    chips = lax.axis_size("z")
    cores = lax.axis_size("core")
    capacity = hidden.shape[3]
    inner_width = hidden.shape[4]
    feature_width = out_grad.shape[1]
    tok_rows = route_ids.shape[0]
    routes = route_ids.shape[1]
    slot_map = slot_table(route_ids, experts, capacity)
    weight_mat = down_weight[0]
    rows_in = hidden[0, 0]
    expert_out = jnp.einsum("sch,hd->scd", rows_in, weight_mat, preferred_element_type=jnp.float32)
    expert_out = expert_out.astype(jnp.bfloat16)
    grads_f = out_grad.astype(jnp.float32)
    by_token = slot_map.reshape(experts, capacity, tok_rows, routes)
    token_hot = jnp.sum(by_token, axis=3)
    slot_gate = jnp.sum(by_token.astype(jnp.float32) * gate_values[None, None], axis=(2, 3))
    slot_grads = jnp.einsum("ect,td->ecd", token_hot, out_grad, preferred_element_type=jnp.float32)
    outgoing = (slot_gate[:, :, None] * slot_grads).astype(jnp.bfloat16)
    grad_rows = lax.all_to_all(outgoing, "expert", split_axis=0, concat_axis=0, tiled=True)
    block = inner_width // (chips * cores)
    c = lax.axis_index("core")
    swap = [(0, 1), (1, 0)]
    col_of = jnp.arange(inner_width, dtype=jnp.int32).reshape(chips, cores, block)

    def columns(core):
        pick = col_of[:, 0, :].reshape(-1) + core * block
        sel = (jnp.arange(inner_width, dtype=jnp.int32)[:, None] == pick[None, :])
        return jnp.einsum(
            "sch,hj->scj", rows_in, sel.astype(jnp.bfloat16), preferred_element_type=jnp.float32
        )

    mine_cols = columns(c).astype(jnp.bfloat16)
    got_cols = lax.ppermute(columns(1 - c).astype(jnp.bfloat16), "core", swap)
    partner = lax.ppermute(grad_rows, "core", swap)
    own_part = jnp.einsum("sch,scd->hd", mine_cols, grad_rows, preferred_element_type=jnp.float32)
    chip_part = own_part + jnp.einsum(
        "sch,scd->hd", got_cols, partner, preferred_element_type=jnp.float32
    )
    weight_grad = lax.psum_scatter(chip_part, "z", scatter_dimension=0, tiled=True)
    returned = lax.all_to_all(expert_out, "expert", split_axis=0, concat_axis=0, tiled=True)
    gathered = jnp.einsum(
        "ecr,ecd->rd",
        slot_map.reshape(experts, capacity, -1),
        returned,
        preferred_element_type=jnp.float32,
    )
    gathered = gathered.reshape(tok_rows, routes, feature_width)
    mixed_out = jnp.sum(gate_values[:, :, None] * gathered, axis=1).astype(jnp.bfloat16)
    gate_grad = jnp.sum(gathered * grads_f[:, None, :], axis=2)
    hidden_grad = jnp.einsum(
        "scd,hd->sch", grad_rows, weight_mat, preferred_element_type=jnp.float32
    )
    hidden_grad = hidden_grad.astype(jnp.bfloat16).reshape(hidden.shape)
    return (mixed_out, gate_grad, hidden_grad, weight_grad[None])


def solution(mesh):
    n_dp = mesh.shape["dp"]
    n_ex = mesh.shape["expert"]
    sub = Mesh(mesh.devices.reshape(n_dp // 2, 2, n_ex), ("z", "core", "expert"))
    tok = ("z", "core", "expert")
    in_specs = (
        P(tok, None),
        P(tok, None),
        P(tok, None),
        P("expert", None, None),
        P(("z", "core"), "expert", None, None, None),
    )
    out_specs = (
        P(tok, None),
        P(tok, None),
        P(("z", "core"), "expert", None, None, None),
        P("expert", ("z", "core"), None),
    )
    return jax.shard_map(
        on_device, mesh=sub, in_specs=in_specs, out_specs=out_specs, check_vma=False
    )
```
